256 devices in a mesh: pair: 32 (over y, x, core), lam: 8 (over z).
Axes of the slice: x: 4, y: 4, z: 8, core: 2. Of those that a mesh axis runs over, the one named last changes fastest.
Arguments:
- integrals: bfloat16 [32, 64, 4, 64, 1024], P('pair', 'lam'), may hold values from -0.119628906 to 0.119628906
- tile_pair: int32 [32, 64], P('pair', 'lam'), may hold values from 0 to 15, as said below
- tile_lam: int32 [32, 64], P('pair', 'lam'), may hold values from 0 to 15, as said below
- tile_count: int32 [32, 8], P('pair', 'lam'), may hold values from 1 to 8, as said below
- mu_index: int32 [2048], P('pair'), may hold values from 0 to 1023
- nu_index: int32 [2048], P('pair'), may hold values from 0 to 1023
- occupied_coef: bfloat16 [1024, 16], replicated, may hold values from -1.5 to 1.5
- virtual_coef: bfloat16 [1024, 1280], replicated, may hold values from -1.5 to 1.5
Outputs:
- orbital_integrals: float32 [16, 1280, 20480], P('lam', 'pair')
The draws below stay inside these ranges and needn't reach their ends.
Inputs may be any that keep to these rules, and one draw needn't show every extreme that they name: On every device the live and dead slots name distinct pairs of (tile_pair, tile_lam); tile_pair lies in 0 to 15. On lam index l every slot's tile_lam lies in l * 2 to (l + 1) * 2 - 1. Slots from tile_count on are dead and their integrals are ignored; some device has all 8 slots live.
All inputs are finite; a program needn't handle non-finite values.
Results may differ from the reference program's by a relative error of at most 0.0049.
Values may be sent and summed in bfloat16 or wider, within the bound.
No kernel may reach another device: no remote copies, remote signals or barrier semaphores. Data moves between devices by JAX's collectives and lax.ppermute only.
A program may use at most 128 MiB of HBM per device.

```python
import jax
import jax.numpy as jnp
from jax import lax

NBF = 1024
OCC = 16
VIR = 1280
BLK = 64
PROWS = 4
TILE_CAP = 8
PB_DEV = 16
PAIR_SHARDS = 32
LAM_SHARDS = 8
LB_DEV = 2
PAIRS = 2048


def tile_lists(key):
    list_key = jax.random.fold_in(key, 11)
    device_keys = jax.random.split(list_key, PAIR_SHARDS * LAM_SHARDS)

    def one_device(device_key):
        chosen = jax.random.permutation(device_key, PB_DEV * LB_DEV)[:TILE_CAP]
        return (chosen // LB_DEV, chosen % LB_DEV)
    pair_blocks, lam_offsets = jax.vmap(one_device)(device_keys)
    pair_blocks = pair_blocks.reshape(PAIR_SHARDS, LAM_SHARDS, TILE_CAP)
    lam_offsets = lam_offsets.reshape(PAIR_SHARDS, LAM_SHARDS, TILE_CAP)
    lam_base = jnp.arange(LAM_SHARDS, dtype=jnp.int32).reshape(1, LAM_SHARDS, 1) * LB_DEV
    lam_blocks = lam_offsets + lam_base
    pair_out = pair_blocks.reshape(PAIR_SHARDS, LAM_SHARDS * TILE_CAP).astype(jnp.int32)
    lam_out = lam_blocks.reshape(PAIR_SHARDS, LAM_SHARDS * TILE_CAP).astype(jnp.int32)
    return (pair_out, lam_out)


def draw_tile_pair(key, part):
    return tile_lists(key)[0]


def draw_tile_lam(key, part):
    return tile_lists(key)[1]


def draw_tile_count(key, part):
    counts = jax.random.randint(jax.random.fold_in(key, 23), (PAIR_SHARDS * LAM_SHARDS,), 1, TILE_CAP + 1)
    busiest = jax.random.randint(jax.random.fold_in(key, 29), (), 0, PAIR_SHARDS * LAM_SHARDS)
    counts = jnp.where(jnp.arange(PAIR_SHARDS * LAM_SHARDS) == busiest, TILE_CAP, counts)
    return counts.reshape(PAIR_SHARDS, LAM_SHARDS).astype(jnp.int32)


def set_ends(values, own_key, low, high):
    index_at = [jax.random.randint(jax.random.fold_in(own_key, axis), (), 0, length) for axis, length in enumerate(values.shape)]
    main_axis = values.shape.index(max(values.shape))
    next_to = index_at[:main_axis] + [(index_at[main_axis] + 1) % values.shape[main_axis]] + index_at[main_axis + 1:]
    return values.at[tuple(index_at)].set(low).at[tuple(next_to)].set(high)


def levels(key, dims, shards, low, largest):
    gain, own = 1.0, jax.random.fold_in(key, 6)
    for position, parts in shards:
        steps = jnp.exp(jax.random.uniform(jax.random.fold_in(own, position), (parts,), jnp.float32, low / len(shards), largest / len(shards)))
        gain = gain * jnp.repeat(steps, dims[position] // parts).reshape([-1 if axis == position else 1 for axis in range(len(dims))])
    return gain


def gaussian(rng, shape, spread, bound, cuts=(), kind=jnp.bfloat16):
    gain = levels(rng, shape, cuts, -0.22, 0.18) if cuts else 1.0
    drawn = jax.random.normal(rng, shape, jnp.float32) * spread * gain
    return jnp.minimum(jnp.maximum(drawn, -bound), bound).astype(kind)


def setup_inputs(seed: int = 0) -> dict:
    keys = jax.random.split(jax.random.key(seed), 9)
    return {
        "integrals": gaussian(keys[0], (PAIR_SHARDS, LAM_SHARDS * TILE_CAP, PROWS, BLK, NBF), 0.02, 0.119628906, ((0, 32), (1, 8))),
        "tile_pair": draw_tile_pair(jax.random.fold_in(keys[8], 71), 0),
        "tile_lam": draw_tile_lam(jax.random.fold_in(keys[8], 71), 0),
        "tile_count": draw_tile_count(jax.random.fold_in(keys[8], 71), 0),
        "mu_index": set_ends(jax.random.randint(keys[4], (PAIRS,), 0, NBF), jax.random.fold_in(keys[4], 1), 0, NBF - 1).astype(jnp.int32),
        "nu_index": set_ends(jax.random.randint(keys[5], (PAIRS,), 0, NBF), jax.random.fold_in(keys[5], 1), 0, NBF - 1).astype(jnp.int32),
        "occupied_coef": gaussian(keys[6], (NBF, OCC), 0.25, 1.5),
        "virtual_coef": gaussian(keys[7], (NBF, VIR), 0.25, 1.5),
    }


def shard_mixed(shard, integrals, tile_pair, tile_lam, tile_count, occ_wide, virtual_coef):
    pair_rows = PB_DEV * PROWS
    tile_data = integrals[shard]
    pair_list = tile_pair[shard]
    lam_list = tile_lam[shard]
    live_counts = tile_count[shard]

    def add_tile(partial_value, slot_index):
        device_slot = slot_index % TILE_CAP
        owner_lam = slot_index // TILE_CAP
        is_live = (device_slot < live_counts[owner_lam]).astype(jnp.float32)
        occ_rows = lax.dynamic_slice_in_dim(occ_wide, (lam_list[slot_index] * BLK).astype(jnp.int32), BLK, 0)
        contrib = jnp.einsum("rls,lj->jrs", tile_data[slot_index].astype(jnp.float32), occ_rows, precision=lax.Precision.HIGHEST)
        row_start = (pair_list[slot_index] * PROWS).astype(jnp.int32)
        current = lax.dynamic_slice_in_dim(partial_value, row_start, PROWS, 1)
        return lax.dynamic_update_slice_in_dim(partial_value, current + is_live * contrib, row_start, 1), None

    start_half = jnp.zeros((OCC, pair_rows, NBF), jnp.float32)
    half, _ = lax.scan(add_tile, start_half, jnp.arange(LAM_SHARDS * TILE_CAP, dtype=jnp.int32))
    half_low = half.astype(jnp.bfloat16)
    mixed = jnp.dot(half_low.reshape(OCC * pair_rows, NBF), virtual_coef, preferred_element_type=jnp.float32)
    return mixed.reshape(OCC, pair_rows, VIR).astype(jnp.bfloat16)


def reference(integrals, tile_pair, tile_lam, tile_count, mu_index, nu_index, occupied_coef, virtual_coef):
    occ_wide = occupied_coef.astype(jnp.float32)
    vir_wide = virtual_coef.astype(jnp.float32)
    pair_rows = PB_DEV * PROWS

    def add_shard(running, shard):
        mixed = shard_mixed(shard, integrals, tile_pair, tile_lam, tile_count, occ_wide, virtual_coef)
        mixed = lax.optimization_barrier(mixed).astype(jnp.float32)
        row_start = (shard * pair_rows).astype(jnp.int32)
        first_rows = lax.dynamic_slice_in_dim(mu_index, row_start, pair_rows)
        second_rows = lax.dynamic_slice_in_dim(nu_index, row_start, pair_rows)
        weights = (occ_wide[first_rows][:, :, None] * vir_wide[second_rows][:, None, :]).astype(jnp.bfloat16)
        weights = lax.optimization_barrier(weights).astype(jnp.float32).reshape(pair_rows, OCC * VIR)
        mixed_rows = jnp.transpose(mixed, (0, 2, 1)).reshape(OCC * VIR, pair_rows)
        return running + jnp.dot(mixed_rows, weights, precision=lax.Precision.HIGHEST), None

    start_total = jnp.zeros((OCC * VIR, OCC * VIR), jnp.float32)
    total, _ = lax.scan(add_shard, start_total, jnp.arange(PAIR_SHARDS, dtype=jnp.int32))
    return total.reshape(OCC, VIR, OCC * VIR)
```

```python
import jax
import jax.numpy as jnp
from jax import lax
from jax.sharding import PartitionSpec as P


def on_device(
    integrals, tile_pair, tile_lam, tile_count, mu_index, nu_index, occupied_coef, virtual_coef
):
    lam_count = lax.axis_size("lam")
    pair_count = lax.axis_size("pair")
    basis_count, occ_total = occupied_coef.shape
    vir_total = virtual_coef.shape[1]
    rows_here = mu_index.shape[0]

    both_index = lax.all_gather(
        jnp.stack([mu_index, nu_index]), "pair", axis=1, tiled=True
    )

    tile_data = integrals[0]
    slot_count, tile_rows, tile_depth, _ = tile_data.shape
    block_count = rows_here // tile_rows
    pair_list = tile_pair[0]
    lam_list = tile_lam[0]
    live = jnp.arange(slot_count) < tile_count[0, 0]
    occ_blocks = occupied_coef.reshape(basis_count // tile_depth, tile_depth, occ_total)
    occ_slot = jnp.take(occ_blocks, lam_list, axis=0)
    hit = (pair_list[:, None] == jnp.arange(block_count)[None, :]) & live[:, None]
    mask = jnp.where(hit[:, :, None, None], occ_slot[:, None, :, :], jnp.zeros((), occ_slot.dtype))
    partial_value = jnp.einsum(
        "tgmj,tkms->jgks", mask, tile_data, preferred_element_type=jnp.float32
    ).reshape(occ_total, rows_here, basis_count)

    own_half = lax.psum_scatter(partial_value, "lam", scatter_dimension=0, tiled=True)
    occ_share = own_half.shape[0]
    vir_share = vir_total // pair_count
    half_low = own_half.astype(jnp.bfloat16).reshape(occ_share * rows_here, basis_count)
    mixed = jnp.dot(half_low, virtual_coef, preferred_element_type=jnp.float32)
    mixed = mixed.astype(jnp.bfloat16).reshape(occ_share, rows_here, pair_count, vir_share)
    received = lax.all_to_all(mixed, "pair", split_axis=2, concat_axis=1, tiled=True)
    total_rows = received.shape[1]
    mixed_rows = received.reshape(occ_share, total_rows, vir_share)

    occ_rows = jnp.take(occupied_coef, both_index[0], axis=0)
    vir_rows = jnp.take(virtual_coef, both_index[1], axis=0)
    scaled = (
        mixed_rows.astype(jnp.float32)[:, :, :, None]
        * occ_rows.astype(jnp.float32)[None, :, None, :]
    ).astype(jnp.bfloat16)
    result = jnp.einsum("qrbi,ra->qbia", scaled, vir_rows, preferred_element_type=jnp.float32)
    return result.reshape(occ_share, vir_share, occ_total * vir_total)


def solution(mesh):
    placed = (
        P("pair", "lam", None, None, None),
        P("pair", "lam"),
        P("pair", "lam"),
        P("pair", "lam"),
        P("pair"),
        P("pair"),
        P(),
        P(),
    )
    return jax.shard_map(
        on_device, mesh=mesh, in_specs=placed, out_specs=P("lam", "pair", None), check_vma=False
    )
```

```python
import jax
import jax.numpy as jnp
from jax import lax
from jax.sharding import PartitionSpec as P


def on_device(
    integrals, tile_pair, tile_lam, tile_count, mu_index, nu_index, occupied_coef, virtual_coef
):
    lam_count = lax.axis_size("lam")
    pair_count = lax.axis_size("pair")
    basis_count, occ_total = occupied_coef.shape
    vir_total = virtual_coef.shape[1]
    rows_here = mu_index.shape[0]

    index_copies = jnp.broadcast_to(
        jnp.stack([mu_index, nu_index])[None], (pair_count, 2, rows_here)
    )
    both_index = lax.all_to_all(index_copies, "pair", split_axis=0, concat_axis=0, tiled=True)
    both_index = jnp.transpose(both_index, (1, 0, 2)).reshape(2, pair_count * rows_here)

    tile_data = integrals[0]
    slot_count, tile_rows, tile_depth, _ = tile_data.shape
    block_count = rows_here // tile_rows
    pair_list = tile_pair[0]
    lam_list = tile_lam[0]
    live = jnp.arange(slot_count) < tile_count[0, 0]
    occ_blocks = occupied_coef.reshape(basis_count // tile_depth, tile_depth, occ_total)
    occ_slot = jnp.take(occ_blocks, lam_list, axis=0)
    hit = (pair_list[:, None] == jnp.arange(block_count)[None, :]) & live[:, None]
    mask = jnp.where(hit[:, :, None, None], occ_slot[:, None, :, :], jnp.zeros((), occ_slot.dtype))
    partial_value = jnp.einsum(
        "tgmj,tkms->jgks", mask, tile_data, preferred_element_type=jnp.float32
    ).reshape(occ_total, rows_here, basis_count)

    own_half = lax.psum_scatter(
        partial_value.astype(jnp.bfloat16), "lam", scatter_dimension=0, tiled=True
    )
    occ_share = own_half.shape[0]
    vir_share = vir_total // pair_count
    half_low = own_half.astype(jnp.bfloat16).reshape(occ_share * rows_here, basis_count)
    mixed = jnp.dot(half_low, virtual_coef, preferred_element_type=jnp.float32)
    mixed = mixed.astype(jnp.bfloat16).reshape(occ_share, rows_here, pair_count, vir_share)
    received = lax.all_to_all(mixed, "pair", split_axis=2, concat_axis=1, tiled=True)
    total_rows = received.shape[1]
    mixed_rows = received.reshape(occ_share, total_rows, vir_share)

    occ_rows = jnp.take(occupied_coef, both_index[0], axis=0)
    vir_rows = jnp.take(virtual_coef, both_index[1], axis=0)
    scaled = (
        mixed_rows.astype(jnp.float32)[:, :, :, None]
        * occ_rows.astype(jnp.float32)[None, :, None, :]
    ).astype(jnp.bfloat16)
    result = jnp.einsum("qrbi,ra->qbia", scaled, vir_rows, preferred_element_type=jnp.float32)
    return result.reshape(occ_share, vir_share, occ_total * vir_total)


def solution(mesh):
    placed = (
        P("pair", "lam", None, None, None),
        P("pair", "lam"),
        P("pair", "lam"),
        P("pair", "lam"),
        P("pair"),
        P("pair"),
        P(),
        P(),
    )
    return jax.shard_map(
        on_device, mesh=mesh, in_specs=placed, out_specs=P("lam", "pair", None), check_vma=False
    )
```

```python
import jax
import jax.numpy as jnp
from jax import lax
from jax.sharding import PartitionSpec as P


def on_device(
    integrals, tile_pair, tile_lam, tile_count, mu_index, nu_index, occupied_coef, virtual_coef
):
    lam_count = lax.axis_size("lam")
    pair_count = lax.axis_size("pair")
    basis_count, occ_total = occupied_coef.shape
    vir_total = virtual_coef.shape[1]
    rows_here = mu_index.shape[0]

    index_copies = jnp.broadcast_to(
        jnp.stack([mu_index, nu_index])[None], (pair_count, 2, rows_here)
    )
    both_index = lax.all_to_all(index_copies, "pair", split_axis=0, concat_axis=0, tiled=True)
    both_index = jnp.transpose(both_index, (1, 0, 2)).reshape(2, pair_count * rows_here)

    tile_data = integrals[0]
    slot_count, tile_rows, tile_depth, _ = tile_data.shape
    block_count = rows_here // tile_rows
    pair_list = tile_pair[0]
    lam_list = tile_lam[0]
    live = jnp.arange(slot_count) < tile_count[0, 0]
    occ_blocks = occupied_coef.reshape(basis_count // tile_depth, tile_depth, occ_total)
    occ_slot = jnp.take(occ_blocks, lam_list, axis=0)
    occ_slot = jnp.where(live[:, None, None], occ_slot, jnp.zeros((), occ_slot.dtype))
    contrib = jnp.einsum("tmj,tkms->jtks", occ_slot, tile_data, preferred_element_type=jnp.float32)
    occ_share = occ_total // lam_count
    contrib = contrib.astype(jnp.bfloat16).reshape(
        lam_count, occ_share, slot_count, tile_rows, basis_count
    )
    pair_or_dead = jnp.where(live, pair_list, -1)
    pair_copies = jnp.broadcast_to(pair_or_dead[None], (lam_count, slot_count))
    pair_all = lax.all_to_all(pair_copies, "lam", split_axis=0, concat_axis=0, tiled=True)
    got = lax.all_to_all(contrib, "lam", split_axis=0, concat_axis=0, tiled=True)
    hit = (pair_all[:, :, None] == jnp.arange(block_count)[None, None, :]).astype(jnp.bfloat16)
    own_half = jnp.einsum(
        "ptg,pjtks->jgks", hit, got, preferred_element_type=jnp.float32
    ).reshape(occ_share, rows_here, basis_count)
    vir_share = vir_total // pair_count
    half_low = own_half.astype(jnp.bfloat16).reshape(occ_share * rows_here, basis_count)
    mixed = jnp.dot(half_low, virtual_coef, preferred_element_type=jnp.float32)
    mixed = mixed.astype(jnp.bfloat16).reshape(occ_share, rows_here, pair_count, vir_share)
    received = lax.all_to_all(mixed, "pair", split_axis=2, concat_axis=1, tiled=True)
    total_rows = received.shape[1]
    mixed_rows = received.reshape(occ_share, total_rows, vir_share)

    occ_rows = jnp.take(occupied_coef, both_index[0], axis=0)
    vir_rows = jnp.take(virtual_coef, both_index[1], axis=0)
    scaled = (
        mixed_rows.astype(jnp.float32)[:, :, :, None]
        * occ_rows.astype(jnp.float32)[None, :, None, :]
    ).astype(jnp.bfloat16)
    result = jnp.einsum("qrbi,ra->qbia", scaled, vir_rows, preferred_element_type=jnp.float32)
    return result.reshape(occ_share, vir_share, occ_total * vir_total)


def solution(mesh):
    placed = (
        P("pair", "lam", None, None, None),
        P("pair", "lam"),
        P("pair", "lam"),
        P("pair", "lam"),
        P("pair"),
        P("pair"),
        P(),
        P(),
    )
    return jax.shard_map(
        on_device, mesh=mesh, in_specs=placed, out_specs=P("lam", "pair", None), check_vma=False
    )
```

```python
import jax
import jax.numpy as jnp
from jax import lax
from jax.sharding import PartitionSpec as P


def on_device(
    integrals, tile_pair, tile_lam, tile_count, mu_index, nu_index, occupied_coef, virtual_coef
):
    lam_count = lax.axis_size("lam")
    pair_count = lax.axis_size("pair")
    basis_count, occ_total = occupied_coef.shape
    vir_total = virtual_coef.shape[1]
    rows_here = mu_index.shape[0]

    index_copies = jnp.broadcast_to(
        jnp.stack([mu_index, nu_index])[None], (pair_count, 2, rows_here)
    )
    both_index = lax.all_to_all(index_copies, "pair", split_axis=0, concat_axis=0, tiled=True)
    both_index = jnp.transpose(both_index, (1, 0, 2)).reshape(2, pair_count * rows_here)

    tile_data = integrals[0]
    slot_count, tile_rows, tile_depth, _ = tile_data.shape
    block_count = rows_here // tile_rows
    pair_list = tile_pair[0]
    lam_list = tile_lam[0]
    live = jnp.arange(slot_count) < tile_count[0, 0]
    occ_blocks = occupied_coef.reshape(basis_count // tile_depth, tile_depth, occ_total)
    occ_slot = jnp.take(occ_blocks, lam_list, axis=0)
    hit = (pair_list[:, None] == jnp.arange(block_count)[None, :]) & live[:, None]
    mask = jnp.where(hit[:, :, None, None], occ_slot[:, None, :, :], jnp.zeros((), occ_slot.dtype))
    occ_share = occ_total // lam_count
    mask = mask.reshape(slot_count, block_count, tile_depth, lam_count, occ_share)
    partial_value = jnp.einsum(
        "tgmlc,tkms->clgks", mask, tile_data, preferred_element_type=jnp.float32
    ).reshape(occ_share, lam_count, rows_here, basis_count)

    occ_rows = jnp.take(occupied_coef, both_index[0], axis=0).astype(jnp.float32)
    vir_rows = jnp.take(virtual_coef, both_index[1], axis=0)
    vir_share = vir_total // pair_count

    pieces = []
    for part in range(occ_share):
        own_half = lax.psum_scatter(partial_value[part], "lam", scatter_dimension=0, tiled=True)
        if pieces:
            pieces[-1], own_half = lax.optimization_barrier((pieces[-1], own_half))
        half_low = own_half.astype(jnp.bfloat16).reshape(rows_here, basis_count)
        mixed = jnp.dot(half_low, virtual_coef, preferred_element_type=jnp.float32)
        mixed = mixed.astype(jnp.bfloat16).reshape(rows_here, pair_count, vir_share)
        received = lax.all_to_all(mixed, "pair", split_axis=1, concat_axis=0, tiled=True)
        mixed_rows = received.reshape(pair_count * rows_here, vir_share)
        scaled = (
            mixed_rows.astype(jnp.float32)[:, :, None] * occ_rows[:, None, :]
        ).astype(jnp.bfloat16)
        pieces.append(
            jnp.einsum("rbi,ra->bia", scaled, vir_rows, preferred_element_type=jnp.float32)
        )
    result = jnp.stack(pieces)
    return result.reshape(occ_share, vir_share, occ_total * vir_total)


def solution(mesh):
    placed = (
        P("pair", "lam", None, None, None),
        P("pair", "lam"),
        P("pair", "lam"),
        P("pair", "lam"),
        P("pair"),
        P("pair"),
        P(),
        P(),
    )
    return jax.shard_map(
        on_device, mesh=mesh, in_specs=placed, out_specs=P("lam", "pair", None), check_vma=False
    )
```

```python
import jax
import jax.numpy as jnp
from jax import lax
from jax.sharding import PartitionSpec as P


def on_device(
    integrals, tile_pair, tile_lam, tile_count, mu_index, nu_index, occupied_coef, virtual_coef
):
    lam_count = lax.axis_size("lam")
    pair_count = lax.axis_size("pair")
    basis_count, occ_total = occupied_coef.shape
    vir_total = virtual_coef.shape[1]
    rows_here = mu_index.shape[0]
    occ_share = occ_total // lam_count
    vir_share = vir_total // pair_count

    tile_data = integrals[0]
    slot_count, tile_rows, tile_depth, _ = tile_data.shape
    block_count = rows_here // tile_rows
    pair_list = tile_pair[0]
    lam_list = tile_lam[0]
    live = jnp.arange(slot_count) < tile_count[0, 0]
    occ_blocks = occupied_coef.reshape(basis_count // tile_depth, tile_depth, occ_total)
    occ_slot = jnp.take(occ_blocks, lam_list, axis=0)
    occ_slot = jnp.where(live[:, None, None], occ_slot, jnp.zeros((), occ_slot.dtype))
    contrib = jnp.einsum("tmj,tkms->jtks", occ_slot, tile_data, preferred_element_type=jnp.float32)

    peak = jnp.maximum(jnp.max(jnp.abs(contrib)), 1e-30)
    exponent = jnp.clip(jnp.floor(jnp.log2(peak)), -100.0, 100.0)
    scale = jnp.exp2(13.0 - exponent)
    payload = (contrib * scale).astype(jnp.float16).reshape(
        lam_count, occ_share, slot_count, tile_rows, basis_count
    )
    hit = (pair_list[:, None] == jnp.arange(block_count)[None, :]) & live[:, None]
    info = jnp.zeros((slot_count, 128), jnp.float32)
    info = info.at[:, :block_count].set(hit.astype(jnp.float32))
    info = info.at[:, block_count].set(exponent)
    info = jnp.broadcast_to(
        info.astype(jnp.float16)[None, None, :, None, :],
        (lam_count, occ_share, slot_count, tile_rows, 128),
    )
    payload = jnp.concatenate([payload, info], axis=4)

    index_copies = jnp.broadcast_to(
        jnp.stack([mu_index, nu_index])[None], (pair_count, 2, rows_here)
    )
    payload, index_copies = lax.optimization_barrier((payload, index_copies))
    got = lax.all_to_all(payload, "lam", split_axis=0, concat_axis=0, tiled=True)
    both_index = lax.all_to_all(index_copies, "pair", split_axis=0, concat_axis=0, tiled=True)
    both_index = jnp.transpose(both_index, (1, 0, 2)).reshape(2, pair_count * rows_here)

    got_info = got[:, 0, :, 0, basis_count:].astype(jnp.float32)
    unscale = jnp.exp2(got_info[:, 0, block_count] - 13.0)
    got_hit = got_info[:, :, :block_count] * unscale[:, None, None]
    own_half = jnp.einsum(
        "ptg,pjtks->jgks",
        got_hit,
        got[..., :basis_count].astype(jnp.float32),
        precision=lax.Precision.HIGHEST,
        preferred_element_type=jnp.float32,
    ).reshape(occ_share, rows_here, basis_count)

    half_low = own_half.astype(jnp.bfloat16).reshape(occ_share * rows_here, basis_count)
    mixed = jnp.dot(half_low, virtual_coef, preferred_element_type=jnp.float32)
    mixed = mixed.astype(jnp.bfloat16).reshape(occ_share, rows_here, pair_count, vir_share)
    received = lax.all_to_all(mixed, "pair", split_axis=2, concat_axis=1, tiled=True)
    total_rows = received.shape[1]
    mixed_rows = received.reshape(occ_share, total_rows, vir_share)

    occ_rows = jnp.take(occupied_coef, both_index[0], axis=0)
    vir_rows = jnp.take(virtual_coef, both_index[1], axis=0)
    scaled = (
        mixed_rows.astype(jnp.float32)[:, :, :, None]
        * occ_rows.astype(jnp.float32)[None, :, None, :]
    ).astype(jnp.bfloat16)
    result = jnp.einsum("qrbi,ra->qbia", scaled, vir_rows, preferred_element_type=jnp.float32)
    return result.reshape(occ_share, vir_share, occ_total * vir_total)


def solution(mesh):
    placed = (
        P("pair", "lam", None, None, None),
        P("pair", "lam"),
        P("pair", "lam"),
        P("pair", "lam"),
        P("pair"),
        P("pair"),
        P(),
        P(),
    )
    return jax.shard_map(
        on_device, mesh=mesh, in_specs=placed, out_specs=P("lam", "pair", None), check_vma=False
    )
```

```python
import jax
import jax.numpy as jnp
from jax import lax
from jax.sharding import PartitionSpec as P


def on_device(
    integrals, tile_pair, tile_lam, tile_count, mu_index, nu_index, occupied_coef, virtual_coef
):
    lam_count = lax.axis_size("lam")
    pair_count = lax.axis_size("pair")
    basis_count, occ_total = occupied_coef.shape
    vir_total = virtual_coef.shape[1]
    rows_here = mu_index.shape[0]
    occ_share = occ_total // lam_count
    vir_share = vir_total // pair_count

    tile_data = integrals[0]
    slot_count, tile_rows, tile_depth, _ = tile_data.shape
    block_count = rows_here // tile_rows
    pair_list = tile_pair[0]
    lam_list = tile_lam[0]
    live = jnp.arange(slot_count) < tile_count[0, 0]
    occ_blocks = occupied_coef.reshape(basis_count // tile_depth, tile_depth, occ_total)
    occ_slot = jnp.take(occ_blocks, lam_list, axis=0)
    occ_slot = jnp.where(live[:, None, None], occ_slot, jnp.zeros((), occ_slot.dtype))
    contrib = jnp.einsum("tmj,tkms->jtks", occ_slot, tile_data, preferred_element_type=jnp.float32)

    peak = jnp.maximum(jnp.max(jnp.abs(contrib)), 1e-30)
    exponent = jnp.clip(jnp.floor(jnp.log2(peak)), -100.0, 100.0)
    scale = jnp.exp2(13.0 - exponent)
    payload = (contrib * scale).astype(jnp.float16).reshape(
        lam_count, occ_share, slot_count, tile_rows, basis_count
    )
    hit = (pair_list[:, None] == jnp.arange(block_count)[None, :]) & live[:, None]
    info = jnp.zeros((slot_count, 128), jnp.float32)
    info = info.at[:, :block_count].set(hit.astype(jnp.float32))
    info = info.at[:, block_count].set(exponent)
    info = jnp.broadcast_to(
        info.astype(jnp.float16)[None, None, :, None, :],
        (lam_count, occ_share, slot_count, tile_rows, 128),
    )
    payload = jnp.concatenate([payload, info], axis=4)

    own_rows = jnp.zeros((2, pair_count, rows_here), jnp.float32)
    own_rows = lax.dynamic_update_index_in_dim(
        own_rows, jnp.stack([mu_index, nu_index]).astype(jnp.float32)[:, None], lax.axis_index("pair"), 1
    )
    both_index = lax.psum(own_rows, "pair").astype(jnp.int32).reshape(2, pair_count * rows_here)
    got = lax.all_to_all(payload, "lam", split_axis=0, concat_axis=0, tiled=True)

    got_info = got[:, 0, :, 0, basis_count:].astype(jnp.float32)
    unscale = jnp.exp2(got_info[:, 0, block_count] - 13.0)
    got_hit = got_info[:, :, :block_count] * unscale[:, None, None]
    own_half = jnp.einsum(
        "ptg,pjtks->jgks",
        got_hit,
        got[..., :basis_count].astype(jnp.float32),
        precision=lax.Precision.HIGHEST,
        preferred_element_type=jnp.float32,
    ).reshape(occ_share, rows_here, basis_count)

    half_low = own_half.astype(jnp.bfloat16).reshape(occ_share * rows_here, basis_count)
    mixed = jnp.dot(half_low, virtual_coef, preferred_element_type=jnp.float32)
    mixed = mixed.astype(jnp.bfloat16).reshape(occ_share, rows_here, pair_count, vir_share)
    received = lax.all_to_all(mixed, "pair", split_axis=2, concat_axis=1, tiled=True)
    total_rows = received.shape[1]
    mixed_rows = received.reshape(occ_share, total_rows, vir_share)

    occ_rows = jnp.take(occupied_coef, both_index[0], axis=0)
    vir_rows = jnp.take(virtual_coef, both_index[1], axis=0)
    scaled = (
        mixed_rows.astype(jnp.float32)[:, :, :, None]
        * occ_rows.astype(jnp.float32)[None, :, None, :]
    ).astype(jnp.bfloat16)
    result = jnp.einsum("qrbi,ra->qbia", scaled, vir_rows, preferred_element_type=jnp.float32)
    return result.reshape(occ_share, vir_share, occ_total * vir_total)


def solution(mesh):
    placed = (
        P("pair", "lam", None, None, None),
        P("pair", "lam"),
        P("pair", "lam"),
        P("pair", "lam"),
        P("pair"),
        P("pair"),
        P(),
        P(),
    )
    return jax.shard_map(
        on_device, mesh=mesh, in_specs=placed, out_specs=P("lam", "pair", None), check_vma=False
    )
```

```python
import jax
import jax.numpy as jnp
from jax import lax
from jax.sharding import PartitionSpec as P


def on_device(
    integrals, tile_pair, tile_lam, tile_count, mu_index, nu_index, occupied_coef, virtual_coef
):
    lam_count = lax.axis_size("lam")
    pair_count = lax.axis_size("pair")
    basis_count, occ_total = occupied_coef.shape
    vir_total = virtual_coef.shape[1]
    rows_here = mu_index.shape[0]
    occ_share = occ_total // lam_count
    vir_share = vir_total // pair_count

    index_copies = jnp.broadcast_to(
        jnp.stack([mu_index, nu_index])[None], (pair_count, 2, rows_here)
    )
    both_index = lax.all_to_all(index_copies, "pair", split_axis=0, concat_axis=0, tiled=True)
    both_index = jnp.transpose(both_index, (1, 0, 2)).reshape(2, pair_count * rows_here)

    tile_data = integrals[0]
    slot_count, tile_rows, tile_depth, _ = tile_data.shape
    block_count = rows_here // tile_rows
    pair_list = tile_pair[0]
    lam_list = tile_lam[0]
    live = jnp.arange(slot_count) < tile_count[0, 0]
    occ_blocks = occupied_coef.reshape(basis_count // tile_depth, tile_depth, occ_total)
    occ_slot = jnp.take(occ_blocks, lam_list, axis=0)
    occ_slot = jnp.where(live[:, None, None], occ_slot, jnp.zeros((), occ_slot.dtype))
    contrib = jnp.einsum("tmj,tkms->jtks", occ_slot, tile_data, preferred_element_type=jnp.float32)

    peak = jnp.maximum(jnp.max(jnp.abs(contrib)), 1e-30)
    exponent = jnp.clip(jnp.floor(jnp.log2(peak)), -100.0, 100.0)
    scale = jnp.exp2(13.0 - exponent)
    payload = (contrib * scale).astype(jnp.float16).reshape(
        lam_count, occ_share, slot_count, tile_rows, basis_count
    )
    hit = (pair_list[:, None] == jnp.arange(block_count)[None, :]) & live[:, None]
    info = jnp.zeros((slot_count, 128), jnp.float32)
    info = info.at[:, :block_count].set(hit.astype(jnp.float32))
    info = info.at[:, block_count].set(exponent)
    info = jnp.broadcast_to(
        info.astype(jnp.float16)[None, None, :, None, :],
        (lam_count, occ_share, slot_count, tile_rows, 128),
    )
    payload = jnp.concatenate([payload, info], axis=4)

    got = lax.all_to_all(payload, "lam", split_axis=0, concat_axis=0, tiled=True)

    got_info = got[:, 0, :, 0, basis_count:].astype(jnp.float32)
    unscale = jnp.exp2(got_info[:, 0, block_count] - 13.0)
    got_hit = got_info[:, :, :block_count] * unscale[:, None, None]
    own_half = jnp.einsum(
        "ptg,pjtks->jgks",
        got_hit,
        got[..., :basis_count].astype(jnp.float32),
        precision=lax.Precision.HIGHEST,
        preferred_element_type=jnp.float32,
    ).reshape(occ_share, rows_here, basis_count)

    half_low = own_half.astype(jnp.bfloat16).reshape(occ_share * rows_here, basis_count)
    mixed = jnp.dot(half_low, virtual_coef, preferred_element_type=jnp.float32)
    mixed = mixed.astype(jnp.bfloat16).reshape(occ_share, rows_here, pair_count, vir_share)
    received = lax.all_to_all(mixed, "pair", split_axis=2, concat_axis=1, tiled=True)
    total_rows = received.shape[1]
    mixed_rows = received.reshape(occ_share, total_rows, vir_share)

    occ_rows = jnp.take(occupied_coef, both_index[0], axis=0)
    vir_rows = jnp.take(virtual_coef, both_index[1], axis=0)
    scaled = (
        mixed_rows.astype(jnp.float32)[:, :, :, None]
        * occ_rows.astype(jnp.float32)[None, :, None, :]
    ).astype(jnp.bfloat16)
    result = jnp.einsum("qrbi,ra->qbia", scaled, vir_rows, preferred_element_type=jnp.float32)
    return result.reshape(occ_share, vir_share, occ_total * vir_total)


def solution(mesh):
    placed = (
        P("pair", "lam", None, None, None),
        P("pair", "lam"),
        P("pair", "lam"),
        P("pair", "lam"),
        P("pair"),
        P("pair"),
        P(),
        P(),
    )
    return jax.shard_map(
        on_device, mesh=mesh, in_specs=placed, out_specs=P("lam", "pair", None), check_vma=False
    )
```

```python
import jax
import jax.numpy as jnp
from jax import lax
from jax.experimental import pallas as pl
from jax.experimental.pallas import tpu as pltpu
from jax.sharding import PartitionSpec as P


def contract_kernel(mixed_ref, occ_ref, vir_ref, out_ref, stack_ref):
    vir_share = mixed_ref.shape[1]
    occ_total = occ_ref.shape[0]
    vir_total = vir_ref.shape[1]
    mixed_block = mixed_ref[0]
    for i in range(occ_total):
        stack_ref[i * vir_share : (i + 1) * vir_share, :] = mixed_block * occ_ref[i : i + 1, :]
    product = jnp.dot(
        stack_ref[...].astype(jnp.bfloat16), vir_ref[...], preferred_element_type=jnp.float32
    )
    for i in range(occ_total):
        out_ref[0, :, i * vir_total : (i + 1) * vir_total] = product[
            i * vir_share : (i + 1) * vir_share, :
        ]


def final_contract(mixed_t, occ_t, vir_rows, interpret=False):
    occ_share, vir_share, total_rows = mixed_t.shape
    occ_total = occ_t.shape[0]
    vir_total = vir_rows.shape[1]
    return pl.pallas_call(
        contract_kernel,
        grid=(occ_share,),
        in_specs=[
            pl.BlockSpec((1, vir_share, total_rows), lambda n: (n, 0, 0)),
            pl.BlockSpec((occ_total, total_rows), lambda n: (0, 0)),
            pl.BlockSpec((total_rows, vir_total), lambda n: (0, 0)),
        ],
        out_specs=pl.BlockSpec((1, vir_share, occ_total * vir_total), lambda n: (n, 0, 0)),
        out_shape=jax.ShapeDtypeStruct((occ_share, vir_share, occ_total * vir_total), jnp.float32),
        scratch_shapes=[pltpu.VMEM((occ_total * vir_share, total_rows), jnp.float32)],
        interpret=interpret,
    )(mixed_t, occ_t, vir_rows)


def on_device(
    integrals, tile_pair, tile_lam, tile_count, mu_index, nu_index, occupied_coef, virtual_coef
):
    lam_count = lax.axis_size("lam")
    pair_count = lax.axis_size("pair")
    basis_count, occ_total = occupied_coef.shape
    vir_total = virtual_coef.shape[1]
    rows_here = mu_index.shape[0]
    occ_share = occ_total // lam_count
    vir_share = vir_total // pair_count

    index_copies = jnp.broadcast_to(
        jnp.stack([mu_index, nu_index])[None], (pair_count, 2, rows_here)
    )
    both_index = lax.all_to_all(index_copies, "pair", split_axis=0, concat_axis=0, tiled=True)
    both_index = jnp.transpose(both_index, (1, 0, 2)).reshape(2, pair_count * rows_here)

    tile_data = integrals[0]
    slot_count, tile_rows, tile_depth, _ = tile_data.shape
    block_count = rows_here // tile_rows
    pair_list = tile_pair[0]
    lam_list = tile_lam[0]
    live = jnp.arange(slot_count) < tile_count[0, 0]
    occ_blocks = occupied_coef.reshape(basis_count // tile_depth, tile_depth, occ_total)
    occ_slot = jnp.take(occ_blocks, lam_list, axis=0)
    occ_slot = jnp.where(live[:, None, None], occ_slot, jnp.zeros((), occ_slot.dtype))
    contrib = jnp.einsum("tmj,tkms->jtks", occ_slot, tile_data, preferred_element_type=jnp.float32)

    peak = jnp.maximum(jnp.max(jnp.abs(contrib)), 1e-30)
    exponent = jnp.clip(jnp.floor(jnp.log2(peak)), -100.0, 100.0)
    scale = jnp.exp2(13.0 - exponent)
    payload = (contrib * scale).astype(jnp.float16).reshape(
        lam_count, occ_share, slot_count, tile_rows, basis_count
    )
    hit = (pair_list[:, None] == jnp.arange(block_count)[None, :]) & live[:, None]
    info = jnp.zeros((slot_count, 128), jnp.float32)
    info = info.at[:, :block_count].set(hit.astype(jnp.float32))
    info = info.at[:, block_count].set(exponent)
    info = jnp.broadcast_to(
        info.astype(jnp.float16)[None, None, :, None, :],
        (lam_count, occ_share, slot_count, tile_rows, 128),
    )
    payload = jnp.concatenate([payload, info], axis=4)

    got = lax.all_to_all(payload, "lam", split_axis=0, concat_axis=0, tiled=True)

    got_info = got[:, 0, :, 0, basis_count:].astype(jnp.float32)
    unscale = jnp.exp2(got_info[:, 0, block_count] - 13.0)
    got_hit = got_info[:, :, :block_count] * unscale[:, None, None]
    own_half = jnp.einsum(
        "ptg,pjtks->jgks",
        got_hit,
        got[..., :basis_count].astype(jnp.float32),
        precision=lax.Precision.HIGHEST,
        preferred_element_type=jnp.float32,
    ).reshape(occ_share, rows_here, basis_count)

    half_low = own_half.astype(jnp.bfloat16).reshape(occ_share * rows_here, basis_count)
    mixed = jnp.dot(half_low, virtual_coef, preferred_element_type=jnp.float32)
    mixed = mixed.astype(jnp.bfloat16).reshape(occ_share, rows_here, pair_count, vir_share)
    received = lax.all_to_all(mixed, "pair", split_axis=2, concat_axis=1, tiled=True)
    total_rows = received.shape[1]
    mixed_rows = received.reshape(occ_share, total_rows, vir_share)

    occ_rows = jnp.take(occupied_coef, both_index[0], axis=0)
    vir_rows = jnp.take(virtual_coef, both_index[1], axis=0)
    mixed_t = jnp.transpose(mixed_rows, (0, 2, 1)).astype(jnp.float32)
    occ_t = jnp.transpose(occ_rows).astype(jnp.float32)
    return final_contract(mixed_t, occ_t, vir_rows)

def solution(mesh):
    placed = (
        P("pair", "lam", None, None, None),
        P("pair", "lam"),
        P("pair", "lam"),
        P("pair", "lam"),
        P("pair"),
        P("pair"),
        P(),
        P(),
    )
    return jax.shard_map(
        on_device, mesh=mesh, in_specs=placed, out_specs=P("lam", "pair", None), check_vma=False
    )
```

```python
import jax
import jax.numpy as jnp
from jax import lax
from jax.experimental import pallas as pl
from jax.experimental.pallas import tpu as pltpu
from jax.sharding import PartitionSpec as P


def contract_kernel(mixed_ref, occ_ref, vir_ref, out_ref, stack_ref):
    vir_share = mixed_ref.shape[1]
    occ_total = occ_ref.shape[0]
    vir_total = vir_ref.shape[1]
    mixed_block = mixed_ref[0].astype(jnp.float32)
    for i in range(occ_total):
        stack_ref[i * vir_share : (i + 1) * vir_share, :] = mixed_block * occ_ref[i : i + 1, :]
    product = jnp.dot(
        stack_ref[...].astype(jnp.bfloat16), vir_ref[...], preferred_element_type=jnp.float32
    )
    for i in range(occ_total):
        out_ref[0, :, i * vir_total : (i + 1) * vir_total] = product[
            i * vir_share : (i + 1) * vir_share, :
        ]


def final_contract(mixed_t, occ_t, vir_rows, interpret=False):
    occ_share, vir_share, total_rows = mixed_t.shape
    occ_total = occ_t.shape[0]
    vir_total = vir_rows.shape[1]
    return pl.pallas_call(
        contract_kernel,
        grid=(occ_share,),
        in_specs=[
            pl.BlockSpec((1, vir_share, total_rows), lambda n: (n, 0, 0)),
            pl.BlockSpec((occ_total, total_rows), lambda n: (0, 0)),
            pl.BlockSpec((total_rows, vir_total), lambda n: (0, 0)),
        ],
        out_specs=pl.BlockSpec((1, vir_share, occ_total * vir_total), lambda n: (n, 0, 0)),
        out_shape=jax.ShapeDtypeStruct((occ_share, vir_share, occ_total * vir_total), jnp.float32),
        scratch_shapes=[pltpu.VMEM((occ_total * vir_share, total_rows), jnp.float32)],
        interpret=interpret,
    )(mixed_t, occ_t, vir_rows)


def on_device(
    integrals, tile_pair, tile_lam, tile_count, mu_index, nu_index, occupied_coef, virtual_coef
):
    lam_count = lax.axis_size("lam")
    pair_count = lax.axis_size("pair")
    basis_count, occ_total = occupied_coef.shape
    vir_total = virtual_coef.shape[1]
    rows_here = mu_index.shape[0]
    occ_share = occ_total // lam_count
    vir_share = vir_total // pair_count

    index_copies = jnp.broadcast_to(
        jnp.stack([mu_index, nu_index])[None], (pair_count, 2, rows_here)
    )
    both_index = lax.all_to_all(index_copies, "pair", split_axis=0, concat_axis=0, tiled=True)
    both_index = jnp.transpose(both_index, (1, 0, 2)).reshape(2, pair_count * rows_here)

    tile_data = integrals[0]
    slot_count, tile_rows, tile_depth, _ = tile_data.shape
    block_count = rows_here // tile_rows
    pair_list = tile_pair[0]
    lam_list = tile_lam[0]
    live = jnp.arange(slot_count) < tile_count[0, 0]
    occ_blocks = occupied_coef.reshape(basis_count // tile_depth, tile_depth, occ_total)
    occ_slot = jnp.take(occ_blocks, lam_list, axis=0)
    occ_slot = jnp.where(live[:, None, None], occ_slot, jnp.zeros((), occ_slot.dtype))
    contrib = jnp.einsum("tmj,tkms->jtks", occ_slot, tile_data, preferred_element_type=jnp.float32)

    peak = jnp.maximum(jnp.max(jnp.abs(contrib)), 1e-30)
    exponent = jnp.clip(jnp.floor(jnp.log2(peak)), -100.0, 100.0)
    scale = jnp.exp2(13.0 - exponent)
    payload = (contrib * scale).astype(jnp.float16).reshape(
        lam_count, occ_share, slot_count, tile_rows, basis_count
    )
    hit = (pair_list[:, None] == jnp.arange(block_count)[None, :]) & live[:, None]
    info = jnp.zeros((slot_count, 128), jnp.float32)
    info = info.at[:, :block_count].set(hit.astype(jnp.float32))
    info = info.at[:, block_count].set(exponent)
    info = jnp.broadcast_to(
        info.astype(jnp.float16)[None, None, :, None, :],
        (lam_count, occ_share, slot_count, tile_rows, 128),
    )
    payload = jnp.concatenate([payload, info], axis=4)

    got = lax.all_to_all(payload, "lam", split_axis=0, concat_axis=0, tiled=True)

    got_info = got[:, 0, :, 0, basis_count:].astype(jnp.float32)
    unscale = jnp.exp2(got_info[:, 0, block_count] - 13.0)
    got_hit = got_info[:, :, :block_count] * unscale[:, None, None]
    own_half = jnp.einsum(
        "ptg,pjtks->jgks",
        got_hit,
        got[..., :basis_count].astype(jnp.float32),
        precision=lax.Precision.HIGHEST,
        preferred_element_type=jnp.float32,
    ).reshape(occ_share, rows_here, basis_count)

    half_low = own_half.astype(jnp.bfloat16).reshape(occ_share * rows_here, basis_count)
    mixed = jnp.dot(half_low, virtual_coef, preferred_element_type=jnp.float32)
    mixed = mixed.astype(jnp.bfloat16).reshape(occ_share, rows_here, pair_count, vir_share)
    received = lax.all_to_all(mixed, "pair", split_axis=2, concat_axis=1, tiled=True)
    total_rows = received.shape[1]
    mixed_rows = received.reshape(occ_share, total_rows, vir_share)

    occ_rows = jnp.take(occupied_coef, both_index[0], axis=0)
    vir_rows = jnp.take(virtual_coef, both_index[1], axis=0)
    mixed_t = jnp.transpose(mixed_rows, (0, 2, 1))
    occ_t = jnp.transpose(occ_rows).astype(jnp.float32)
    return final_contract(mixed_t, occ_t, vir_rows)

def solution(mesh):
    placed = (
        P("pair", "lam", None, None, None),
        P("pair", "lam"),
        P("pair", "lam"),
        P("pair", "lam"),
        P("pair"),
        P("pair"),
        P(),
        P(),
    )
    return jax.shard_map(
        on_device, mesh=mesh, in_specs=placed, out_specs=P("lam", "pair", None), check_vma=False
    )
```

```python
import jax
import jax.numpy as jnp
from jax import lax
from jax.experimental import pallas as pl
from jax.experimental.pallas import tpu as pltpu
from jax.sharding import PartitionSpec as P


def contract_kernel(mixed_ref, occ_ref, vir_ref, out_ref, stack_ref):
    vir_share = mixed_ref.shape[1]
    occ_total = occ_ref.shape[0]
    vir_total = vir_ref.shape[1]
    mixed_block = mixed_ref[0].astype(jnp.float32)
    for i in range(occ_total):
        stack_ref[i * vir_share : (i + 1) * vir_share, :] = mixed_block * occ_ref[i : i + 1, :]
    product = jnp.dot(
        stack_ref[...].astype(jnp.bfloat16), vir_ref[...], preferred_element_type=jnp.float32
    )
    for i in range(occ_total):
        out_ref[0, :, i * vir_total : (i + 1) * vir_total] = product[
            i * vir_share : (i + 1) * vir_share, :
        ]


def final_contract(mixed_t, occ_t, vir_rows, interpret=False):
    occ_share, vir_share, total_rows = mixed_t.shape
    occ_total = occ_t.shape[0]
    vir_total = vir_rows.shape[1]
    return pl.pallas_call(
        contract_kernel,
        grid=(occ_share,),
        in_specs=[
            pl.BlockSpec((1, vir_share, total_rows), lambda n: (n, 0, 0)),
            pl.BlockSpec((occ_total, total_rows), lambda n: (0, 0)),
            pl.BlockSpec((total_rows, vir_total), lambda n: (0, 0)),
        ],
        out_specs=pl.BlockSpec((1, vir_share, occ_total * vir_total), lambda n: (n, 0, 0)),
        out_shape=jax.ShapeDtypeStruct((occ_share, vir_share, occ_total * vir_total), jnp.float32),
        scratch_shapes=[pltpu.VMEM((occ_total * vir_share, total_rows), jnp.float32)],
        interpret=interpret,
    )(mixed_t, occ_t, vir_rows)


def on_device(
    integrals, tile_pair, tile_lam, tile_count, mu_index, nu_index, occupied_coef, virtual_coef
):
    lam_count = lax.axis_size("lam")
    pair_count = lax.axis_size("pair")
    basis_count, occ_total = occupied_coef.shape
    vir_total = virtual_coef.shape[1]
    rows_here = mu_index.shape[0]
    occ_share = occ_total // lam_count
    vir_share = vir_total // pair_count

    index_copies = jnp.broadcast_to(
        jnp.stack([mu_index, nu_index])[None], (pair_count, 2, rows_here)
    )
    both_index = lax.all_to_all(index_copies, "pair", split_axis=0, concat_axis=0, tiled=True)
    both_index = jnp.transpose(both_index, (1, 0, 2)).reshape(2, pair_count * rows_here)

    tile_data = integrals[0]
    slot_count, tile_rows, tile_depth, _ = tile_data.shape
    block_count = rows_here // tile_rows
    pair_list = tile_pair[0]
    lam_list = tile_lam[0]
    live = jnp.arange(slot_count) < tile_count[0, 0]
    occ_blocks = occupied_coef.reshape(basis_count // tile_depth, tile_depth, occ_total)
    occ_slot = jnp.take(occ_blocks, lam_list, axis=0)
    occ_slot = jnp.where(live[:, None, None], occ_slot, jnp.zeros((), occ_slot.dtype))
    contrib = jnp.einsum("tmj,tkms->jtks", occ_slot, tile_data, preferred_element_type=jnp.float32)

    peak = jnp.maximum(jnp.max(jnp.abs(contrib)), 1e-30)
    exponent = jnp.clip(jnp.floor(jnp.log2(peak)), -100.0, 100.0)
    scale = jnp.exp2(13.0 - exponent)
    payload = (contrib * scale).astype(jnp.float16).reshape(
        lam_count, occ_share, slot_count, tile_rows, basis_count
    )
    hit = (pair_list[:, None] == jnp.arange(block_count)[None, :]) & live[:, None]
    info = jnp.zeros((slot_count, 128), jnp.float32)
    info = info.at[:, :block_count].set(hit.astype(jnp.float32))
    info = info.at[:, block_count].set(exponent)
    info = jnp.broadcast_to(
        info.astype(jnp.float16)[None, None, :, None, :],
        (lam_count, occ_share, slot_count, tile_rows, 128),
    )
    payload = jnp.concatenate([payload, info], axis=4)

    lam_here = lax.axis_index("lam")
    arrived = [lax.dynamic_index_in_dim(payload, lam_here, 0, keepdims=False)]
    for shift in range(1, lam_count):
        outgoing = lax.dynamic_index_in_dim(payload, (lam_here + shift) % lam_count, 0, keepdims=False)
        ring = [(source, (source + shift) % lam_count) for source in range(lam_count)]
        arrived.append(lax.ppermute(outgoing, "lam", ring))
    got = jnp.stack(arrived)

    got_info = got[:, 0, :, 0, basis_count:].astype(jnp.float32)
    unscale = jnp.exp2(got_info[:, 0, block_count] - 13.0)
    got_hit = got_info[:, :, :block_count] * unscale[:, None, None]
    own_half = jnp.einsum(
        "ptg,pjtks->jgks",
        got_hit,
        got[..., :basis_count].astype(jnp.float32),
        precision=lax.Precision.HIGHEST,
        preferred_element_type=jnp.float32,
    ).reshape(occ_share, rows_here, basis_count)

    half_low = own_half.astype(jnp.bfloat16).reshape(occ_share * rows_here, basis_count)
    mixed = jnp.dot(half_low, virtual_coef, preferred_element_type=jnp.float32)
    mixed = mixed.astype(jnp.bfloat16).reshape(occ_share, rows_here, pair_count, vir_share)
    received = lax.all_to_all(mixed, "pair", split_axis=2, concat_axis=1, tiled=True)
    total_rows = received.shape[1]
    mixed_rows = received.reshape(occ_share, total_rows, vir_share)

    occ_rows = jnp.take(occupied_coef, both_index[0], axis=0)
    vir_rows = jnp.take(virtual_coef, both_index[1], axis=0)
    mixed_t = jnp.transpose(mixed_rows, (0, 2, 1))
    occ_t = jnp.transpose(occ_rows).astype(jnp.float32)
    return final_contract(mixed_t, occ_t, vir_rows)

def solution(mesh):
    placed = (
        P("pair", "lam", None, None, None),
        P("pair", "lam"),
        P("pair", "lam"),
        P("pair", "lam"),
        P("pair"),
        P("pair"),
        P(),
        P(),
    )
    return jax.shard_map(
        on_device, mesh=mesh, in_specs=placed, out_specs=P("lam", "pair", None), check_vma=False
    )
```

```python
import jax
import jax.numpy as jnp
from jax import lax
from jax.experimental import pallas as pl
from jax.experimental.pallas import tpu as pltpu
from jax.sharding import PartitionSpec as P


def contract_kernel(mixed_ref, occ_ref, vir_ref, out_ref, stack_ref):
    vir_share = mixed_ref.shape[1]
    occ_total = occ_ref.shape[0]
    vir_total = vir_ref.shape[1]
    mixed_block = mixed_ref[0].astype(jnp.float32)
    for i in range(0, occ_total, 2):
        pair_rows = jnp.concatenate(
            [mixed_block * occ_ref[i : i + 1, :], mixed_block * occ_ref[i + 1 : i + 2, :]], axis=0
        )
        stack_ref[i * vir_share : (i + 2) * vir_share, :] = pair_rows.astype(jnp.bfloat16)
    product = jnp.dot(stack_ref[...], vir_ref[...], preferred_element_type=jnp.float32)
    for i in range(occ_total):
        out_ref[0, :, i * vir_total : (i + 1) * vir_total] = product[
            i * vir_share : (i + 1) * vir_share, :
        ]


def final_contract(mixed_t, occ_t, vir_rows, interpret=False):
    occ_share, vir_share, total_rows = mixed_t.shape
    occ_total = occ_t.shape[0]
    vir_total = vir_rows.shape[1]
    return pl.pallas_call(
        contract_kernel,
        grid=(occ_share,),
        in_specs=[
            pl.BlockSpec((1, vir_share, total_rows), lambda n: (n, 0, 0)),
            pl.BlockSpec((occ_total, total_rows), lambda n: (0, 0)),
            pl.BlockSpec((total_rows, vir_total), lambda n: (0, 0)),
        ],
        out_specs=pl.BlockSpec((1, vir_share, occ_total * vir_total), lambda n: (n, 0, 0)),
        out_shape=jax.ShapeDtypeStruct((occ_share, vir_share, occ_total * vir_total), jnp.float32),
        scratch_shapes=[pltpu.VMEM((occ_total * vir_share, total_rows), jnp.bfloat16)],
        interpret=interpret,
    )(mixed_t, occ_t, vir_rows)


def on_device(
    integrals, tile_pair, tile_lam, tile_count, mu_index, nu_index, occupied_coef, virtual_coef
):
    lam_count = lax.axis_size("lam")
    pair_count = lax.axis_size("pair")
    basis_count, occ_total = occupied_coef.shape
    vir_total = virtual_coef.shape[1]
    rows_here = mu_index.shape[0]
    occ_share = occ_total // lam_count
    vir_share = vir_total // pair_count

    index_copies = jnp.broadcast_to(
        jnp.stack([mu_index, nu_index])[None], (pair_count, 2, rows_here)
    )
    both_index = lax.all_to_all(index_copies, "pair", split_axis=0, concat_axis=0, tiled=True)
    both_index = jnp.transpose(both_index, (1, 0, 2)).reshape(2, pair_count * rows_here)

    tile_data = integrals[0]
    slot_count, tile_rows, tile_depth, _ = tile_data.shape
    block_count = rows_here // tile_rows
    pair_list = tile_pair[0]
    lam_list = tile_lam[0]
    live = jnp.arange(slot_count) < tile_count[0, 0]
    occ_blocks = occupied_coef.reshape(basis_count // tile_depth, tile_depth, occ_total)
    occ_slot = jnp.take(occ_blocks, lam_list, axis=0)
    occ_slot = jnp.where(live[:, None, None], occ_slot, jnp.zeros((), occ_slot.dtype))
    contrib = jnp.einsum("tmj,tkms->jtks", occ_slot, tile_data, preferred_element_type=jnp.float32)

    peak = jnp.maximum(jnp.max(jnp.abs(contrib)), 1e-30)
    exponent = jnp.clip(jnp.floor(jnp.log2(peak)), -100.0, 100.0)
    scale = jnp.exp2(13.0 - exponent)
    payload = (contrib * scale).astype(jnp.float16).reshape(
        lam_count, occ_share, slot_count, tile_rows, basis_count
    )
    hit = (pair_list[:, None] == jnp.arange(block_count)[None, :]) & live[:, None]
    info = jnp.zeros((slot_count, 128), jnp.float32)
    info = info.at[:, :block_count].set(hit.astype(jnp.float32))
    info = info.at[:, block_count].set(exponent)
    info = jnp.broadcast_to(
        info.astype(jnp.float16)[None, None, :, None, :],
        (lam_count, occ_share, slot_count, tile_rows, 128),
    )
    payload = jnp.concatenate([payload, info], axis=4)

    got = lax.all_to_all(payload, "lam", split_axis=0, concat_axis=0, tiled=True)

    got_info = got[:, 0, :, 0, basis_count:].astype(jnp.float32)
    unscale = jnp.exp2(got_info[:, 0, block_count] - 13.0)
    got_hit = got_info[:, :, :block_count] * unscale[:, None, None]
    own_half = jnp.einsum(
        "ptg,pjtks->jgks",
        got_hit,
        got[..., :basis_count].astype(jnp.float32),
        precision=lax.Precision.HIGHEST,
        preferred_element_type=jnp.float32,
    ).reshape(occ_share, rows_here, basis_count)

    half_low = own_half.astype(jnp.bfloat16).reshape(occ_share * rows_here, basis_count)
    mixed = jnp.dot(half_low, virtual_coef, preferred_element_type=jnp.float32)
    mixed = mixed.astype(jnp.bfloat16).reshape(occ_share, rows_here, pair_count, vir_share)
    received = lax.all_to_all(mixed, "pair", split_axis=2, concat_axis=1, tiled=True)
    total_rows = received.shape[1]
    mixed_rows = received.reshape(occ_share, total_rows, vir_share)

    occ_rows = jnp.take(occupied_coef, both_index[0], axis=0)
    vir_rows = jnp.take(virtual_coef, both_index[1], axis=0)
    mixed_t = jnp.transpose(mixed_rows, (0, 2, 1))
    occ_t = jnp.transpose(occ_rows).astype(jnp.float32)
    return final_contract(mixed_t, occ_t, vir_rows)

def solution(mesh):
    placed = (
        P("pair", "lam", None, None, None),
        P("pair", "lam"),
        P("pair", "lam"),
        P("pair", "lam"),
        P("pair"),
        P("pair"),
        P(),
        P(),
    )
    return jax.shard_map(
        on_device, mesh=mesh, in_specs=placed, out_specs=P("lam", "pair", None), check_vma=False
    )
```

```python
import jax
import jax.numpy as jnp
from jax import lax
from jax.experimental import pallas as pl
from jax.experimental.pallas import tpu as pltpu
from jax.sharding import PartitionSpec as P


def contract_kernel(mixed_ref, occ_ref, vir_ref, out_ref, stack_ref):
    vir_share = mixed_ref.shape[1]
    occ_total = occ_ref.shape[0]
    vir_total = vir_ref.shape[1]
    mixed_block = mixed_ref[0].astype(jnp.float32)
    for i in range(occ_total):
        stack_ref[i * vir_share : (i + 1) * vir_share, :] = mixed_block * occ_ref[i : i + 1, :]
    product = jnp.dot(
        stack_ref[...].astype(jnp.bfloat16), vir_ref[...], preferred_element_type=jnp.float32
    )
    for i in range(occ_total):
        out_ref[0, :, i * vir_total : (i + 1) * vir_total] = product[
            i * vir_share : (i + 1) * vir_share, :
        ]


def final_contract(mixed_t, occ_t, vir_rows, interpret=False):
    occ_share, vir_share, total_rows = mixed_t.shape
    occ_total = occ_t.shape[0]
    vir_total = vir_rows.shape[1]
    return pl.pallas_call(
        contract_kernel,
        grid=(occ_share,),
        in_specs=[
            pl.BlockSpec((1, vir_share, total_rows), lambda n: (n, 0, 0)),
            pl.BlockSpec((occ_total, total_rows), lambda n: (0, 0)),
            pl.BlockSpec((total_rows, vir_total), lambda n: (0, 0)),
        ],
        out_specs=pl.BlockSpec((1, vir_share, occ_total * vir_total), lambda n: (n, 0, 0)),
        out_shape=jax.ShapeDtypeStruct((occ_share, vir_share, occ_total * vir_total), jnp.float32),
        scratch_shapes=[pltpu.VMEM((occ_total * vir_share, total_rows), jnp.float32)],
        interpret=interpret,
    )(mixed_t, occ_t, vir_rows)


def on_device(
    integrals, tile_pair, tile_lam, tile_count, mu_index, nu_index, occupied_coef, virtual_coef
):
    lam_count = lax.axis_size("lam")
    pair_count = lax.axis_size("pair")
    basis_count, occ_total = occupied_coef.shape
    vir_total = virtual_coef.shape[1]
    rows_here = mu_index.shape[0]
    occ_share = occ_total // lam_count
    vir_share = vir_total // pair_count

    index_copies = jnp.broadcast_to(
        jnp.stack([mu_index, nu_index])[None], (pair_count, 2, rows_here)
    )
    both_index = lax.all_to_all(index_copies, "pair", split_axis=0, concat_axis=0, tiled=True)
    both_index = jnp.transpose(both_index, (1, 0, 2)).reshape(2, pair_count * rows_here)

    tile_data = integrals[0]
    slot_count, tile_rows, tile_depth, _ = tile_data.shape
    block_count = rows_here // tile_rows
    pair_list = tile_pair[0]
    lam_list = tile_lam[0]
    live = jnp.arange(slot_count) < tile_count[0, 0]
    occ_blocks = occupied_coef.reshape(basis_count // tile_depth, tile_depth, occ_total)
    occ_slot = jnp.take(occ_blocks, lam_list, axis=0, mode="clip")
    occ_slot = jnp.where(live[:, None, None], occ_slot, jnp.zeros((), occ_slot.dtype))
    contrib = jnp.einsum("tmj,tkms->jtks", occ_slot, tile_data, preferred_element_type=jnp.float32)

    peak = jnp.maximum(jnp.max(jnp.abs(contrib)), 1e-30)
    exponent = jnp.clip(jnp.floor(jnp.log2(peak)), -100.0, 100.0)
    scale = jnp.exp2(13.0 - exponent)
    payload = (contrib * scale).astype(jnp.float16).reshape(
        lam_count, occ_share, slot_count, tile_rows, basis_count
    )
    hit = (pair_list[:, None] == jnp.arange(block_count)[None, :]) & live[:, None]
    info = jnp.zeros((slot_count, 128), jnp.float32)
    info = info.at[:, :block_count].set(hit.astype(jnp.float32))
    info = info.at[:, block_count].set(exponent)
    info = jnp.broadcast_to(
        info.astype(jnp.float16)[None, None, :, None, :],
        (lam_count, occ_share, slot_count, tile_rows, 128),
    )
    payload = jnp.concatenate([payload, info], axis=4)

    got = lax.all_to_all(payload, "lam", split_axis=0, concat_axis=0, tiled=True)

    got_info = got[:, 0, :, 0, basis_count:].astype(jnp.float32)
    unscale = jnp.exp2(got_info[:, 0, block_count] - 13.0)
    got_hit = got_info[:, :, :block_count] * unscale[:, None, None]
    own_half = jnp.einsum(
        "ptg,pjtks->jgks",
        got_hit,
        got[..., :basis_count].astype(jnp.float32),
        precision=lax.Precision.HIGHEST,
        preferred_element_type=jnp.float32,
    ).reshape(occ_share, rows_here, basis_count)

    half_low = own_half.astype(jnp.bfloat16).reshape(occ_share * rows_here, basis_count)
    mixed = jnp.dot(half_low, virtual_coef, preferred_element_type=jnp.float32)
    mixed = mixed.astype(jnp.bfloat16).reshape(occ_share, rows_here, pair_count, vir_share)
    received = lax.all_to_all(mixed, "pair", split_axis=2, concat_axis=1, tiled=True)
    total_rows = received.shape[1]
    mixed_rows = received.reshape(occ_share, total_rows, vir_share)

    occ_rows = jnp.take(occupied_coef, both_index[0], axis=0, mode="clip")
    vir_rows = jnp.take(virtual_coef, both_index[1], axis=0, mode="clip")
    mixed_t = jnp.transpose(mixed_rows, (0, 2, 1))
    occ_t = jnp.transpose(occ_rows).astype(jnp.float32)
    return final_contract(mixed_t, occ_t, vir_rows)

def solution(mesh):
    placed = (
        P("pair", "lam", None, None, None),
        P("pair", "lam"),
        P("pair", "lam"),
        P("pair", "lam"),
        P("pair"),
        P("pair"),
        P(),
        P(),
    )
    return jax.shard_map(
        on_device, mesh=mesh, in_specs=placed, out_specs=P("lam", "pair", None), check_vma=False
    )
```

```python
import jax
import jax.numpy as jnp
from jax import lax
from jax.experimental import pallas as pl
from jax.experimental.pallas import tpu as pltpu
from jax.sharding import PartitionSpec as P


def contract_kernel(mixed_ref, occ_ref, vir_ref, out_ref, stack_ref):
    vir_share = mixed_ref.shape[1]
    occ_total = occ_ref.shape[0]
    vir_total = vir_ref.shape[1]
    mixed_block = mixed_ref[0].astype(jnp.float32)
    for i in range(occ_total):
        stack_ref[i * vir_share : (i + 1) * vir_share, :] = mixed_block * occ_ref[i : i + 1, :]
    product = jnp.dot(
        stack_ref[...].astype(jnp.bfloat16), vir_ref[...], preferred_element_type=jnp.float32
    )
    for i in range(occ_total):
        out_ref[0, :, i * vir_total : (i + 1) * vir_total] = product[
            i * vir_share : (i + 1) * vir_share, :
        ]


def final_contract(mixed_t, occ_t, vir_rows, interpret=False):
    occ_share, vir_share, total_rows = mixed_t.shape
    occ_total = occ_t.shape[0]
    vir_total = vir_rows.shape[1]
    return pl.pallas_call(
        contract_kernel,
        grid=(occ_share,),
        in_specs=[
            pl.BlockSpec((1, vir_share, total_rows), lambda n: (n, 0, 0)),
            pl.BlockSpec((occ_total, total_rows), lambda n: (0, 0)),
            pl.BlockSpec((total_rows, vir_total), lambda n: (0, 0)),
        ],
        out_specs=pl.BlockSpec((1, vir_share, occ_total * vir_total), lambda n: (n, 0, 0)),
        out_shape=jax.ShapeDtypeStruct((occ_share, vir_share, occ_total * vir_total), jnp.float32),
        scratch_shapes=[pltpu.VMEM((occ_total * vir_share, total_rows), jnp.float32)],
        interpret=interpret,
    )(mixed_t, occ_t, vir_rows)


def on_device(
    integrals, tile_pair, tile_lam, tile_count, mu_index, nu_index, occupied_coef, virtual_coef
):
    lam_count = lax.axis_size("lam")
    pair_count = lax.axis_size("pair")
    basis_count, occ_total = occupied_coef.shape
    vir_total = virtual_coef.shape[1]
    rows_here = mu_index.shape[0]
    occ_share = occ_total // lam_count
    vir_share = vir_total // pair_count

    index_copies = jnp.broadcast_to(
        jnp.stack([mu_index, nu_index])[None], (pair_count, 2, rows_here)
    )
    both_index = lax.all_to_all(index_copies, "pair", split_axis=0, concat_axis=0, tiled=True)
    both_index = jnp.transpose(both_index, (1, 0, 2)).reshape(2, pair_count * rows_here)

    tile_data = integrals[0]
    slot_count, tile_rows, tile_depth, _ = tile_data.shape
    block_count = rows_here // tile_rows
    pair_list = tile_pair[0]
    lam_list = tile_lam[0]
    live = jnp.arange(slot_count) < tile_count[0, 0]
    occ_blocks = occupied_coef.reshape(basis_count // tile_depth, tile_depth, occ_total)
    occ_slot = jnp.take(occ_blocks, lam_list, axis=0, mode="clip")
    occ_slot = jnp.where(live[:, None, None], occ_slot, jnp.zeros((), occ_slot.dtype))
    contrib = jnp.einsum("tmj,tkms->jtks", occ_slot, tile_data, preferred_element_type=jnp.float32)

    peak = jnp.maximum(jnp.max(jnp.abs(contrib)), 1e-30)
    exponent = jnp.clip(jnp.floor(jnp.log2(peak)), -100.0, 100.0)
    scale = jnp.exp2(13.0 - exponent)
    payload = (contrib * scale).astype(jnp.float16).reshape(
        lam_count, occ_share, slot_count, tile_rows, basis_count
    )
    hit = (pair_list[:, None] == jnp.arange(block_count)[None, :]) & live[:, None]
    info = jnp.zeros((slot_count, 128), jnp.float32)
    info = info.at[:, :block_count].set(hit.astype(jnp.float32))
    info = info.at[:, block_count].set(exponent)
    info = jnp.broadcast_to(
        info.astype(jnp.float16)[None, None, :, None, :],
        (lam_count, occ_share, slot_count, tile_rows, 128),
    )
    payload = jnp.concatenate([payload, info], axis=4)

    got = lax.all_to_all(payload, "lam", split_axis=0, concat_axis=0, tiled=True)

    got_info = got[:, 0, :, 0, basis_count:].astype(jnp.float32)
    unscale = jnp.exp2(got_info[:, 0, block_count] - 13.0)
    got_hit = got_info[:, :, :block_count] * unscale[:, None, None]
    got_data = got[..., :basis_count].astype(jnp.float32)
    data_high = got_data.astype(jnp.bfloat16)
    data_low = (got_data - data_high.astype(jnp.float32)).astype(jnp.bfloat16)
    hit_weight = got_hit.astype(jnp.bfloat16)
    own_half = jnp.einsum(
        "ptg,pjtks->jgks", hit_weight, data_high, preferred_element_type=jnp.float32
    ) + jnp.einsum("ptg,pjtks->jgks", hit_weight, data_low, preferred_element_type=jnp.float32)

    half_low = own_half.astype(jnp.bfloat16).reshape(occ_share, rows_here, basis_count)
    mixed = jnp.einsum("sn,jrs->njr", virtual_coef, half_low, preferred_element_type=jnp.float32)
    mixed = mixed.astype(jnp.bfloat16).reshape(pair_count, vir_share, occ_share, rows_here)
    received = lax.all_to_all(mixed, "pair", split_axis=0, concat_axis=0, tiled=True)
    mixed_t = jnp.transpose(received, (2, 1, 0, 3)).reshape(
        occ_share, vir_share, pair_count * rows_here
    )

    occ_rows = jnp.take(occupied_coef, both_index[0], axis=0, mode="clip")
    vir_rows = jnp.take(virtual_coef, both_index[1], axis=0, mode="clip")
    occ_t = jnp.transpose(occ_rows).astype(jnp.float32)
    return final_contract(mixed_t, occ_t, vir_rows)

def solution(mesh):
    placed = (
        P("pair", "lam", None, None, None),
        P("pair", "lam"),
        P("pair", "lam"),
        P("pair", "lam"),
        P("pair"),
        P("pair"),
        P(),
        P(),
    )
    return jax.shard_map(
        on_device, mesh=mesh, in_specs=placed, out_specs=P("lam", "pair", None), check_vma=False
    )
```

```python
import jax
import jax.numpy as jnp
from jax import lax
from jax.experimental import pallas as pl
from jax.experimental.pallas import tpu as pltpu
from jax.sharding import PartitionSpec as P


def contract_kernel(mixed_ref, occ_ref, vir_ref, out_ref, stack_ref):
    vir_share = mixed_ref.shape[1]
    occ_total = occ_ref.shape[0]
    vir_total = vir_ref.shape[1]
    mixed_block = mixed_ref[0].astype(jnp.float32)
    for i in range(occ_total):
        stack_ref[i * vir_share : (i + 1) * vir_share, :] = mixed_block * occ_ref[i : i + 1, :]
    product = jnp.dot(
        stack_ref[...].astype(jnp.bfloat16), vir_ref[...], preferred_element_type=jnp.float32
    )
    for i in range(occ_total):
        out_ref[0, :, i * vir_total : (i + 1) * vir_total] = product[
            i * vir_share : (i + 1) * vir_share, :
        ]


def final_contract(mixed_t, occ_t, vir_rows, interpret=False):
    occ_share, vir_share, total_rows = mixed_t.shape
    occ_total = occ_t.shape[0]
    vir_total = vir_rows.shape[1]
    return pl.pallas_call(
        contract_kernel,
        grid=(occ_share,),
        in_specs=[
            pl.BlockSpec((1, vir_share, total_rows), lambda n: (n, 0, 0)),
            pl.BlockSpec((occ_total, total_rows), lambda n: (0, 0)),
            pl.BlockSpec((total_rows, vir_total), lambda n: (0, 0)),
        ],
        out_specs=pl.BlockSpec((1, vir_share, occ_total * vir_total), lambda n: (n, 0, 0)),
        out_shape=jax.ShapeDtypeStruct((occ_share, vir_share, occ_total * vir_total), jnp.float32),
        scratch_shapes=[pltpu.VMEM((occ_total * vir_share, total_rows), jnp.float32)],
        interpret=interpret,
    )(mixed_t, occ_t, vir_rows)


def on_device(
    integrals, tile_pair, tile_lam, tile_count, mu_index, nu_index, occupied_coef, virtual_coef
):
    lam_count = lax.axis_size("lam")
    pair_count = lax.axis_size("pair")
    basis_count, occ_total = occupied_coef.shape
    vir_total = virtual_coef.shape[1]
    rows_here = mu_index.shape[0]
    occ_share = occ_total // lam_count
    vir_share = vir_total // pair_count

    index_copies = jnp.broadcast_to(
        jnp.stack([mu_index, nu_index])[None], (pair_count, 2, rows_here)
    )
    both_index = lax.all_to_all(index_copies, "pair", split_axis=0, concat_axis=0, tiled=True)
    both_index = jnp.transpose(both_index, (1, 0, 2)).reshape(2, pair_count * rows_here)

    tile_data = integrals[0]
    slot_count, tile_rows, tile_depth, _ = tile_data.shape
    block_count = rows_here // tile_rows
    pair_list = tile_pair[0]
    lam_list = tile_lam[0]
    live = jnp.arange(slot_count) < tile_count[0, 0]
    occ_blocks = occupied_coef.reshape(basis_count // tile_depth, tile_depth, occ_total)
    occ_slot = jnp.take(occ_blocks, lam_list, axis=0, mode="clip")
    occ_slot = jnp.where(live[:, None, None], occ_slot, jnp.zeros((), occ_slot.dtype))
    contrib = jnp.einsum("tmj,tkms->jtks", occ_slot, tile_data, preferred_element_type=jnp.float32)

    peak = jnp.maximum(jnp.max(jnp.abs(contrib)), 1e-30)
    exponent = jnp.clip(jnp.floor(jnp.log2(peak)), -100.0, 100.0)
    scale = jnp.exp2(13.0 - exponent)
    payload = (contrib * scale).astype(jnp.float16).reshape(
        lam_count, occ_share, slot_count, tile_rows, basis_count
    )
    hit = (pair_list[:, None] == jnp.arange(block_count)[None, :]) & live[:, None]
    info = jnp.zeros((slot_count, 128), jnp.float32)
    info = info.at[:, :block_count].set(hit.astype(jnp.float32))
    info = info.at[:, block_count].set(exponent)
    info = jnp.broadcast_to(
        info.astype(jnp.float16)[None, None, :, None, :],
        (lam_count, occ_share, slot_count, tile_rows, 128),
    )
    payload = jnp.concatenate([payload, info], axis=4)

    got = lax.all_to_all(payload, "lam", split_axis=0, concat_axis=0, tiled=True)

    got_info = got[:, 0, :, 0, basis_count:].astype(jnp.float32)
    unscale = jnp.exp2(got_info[:, 0, block_count] - 13.0)
    got_hit = got_info[:, :, :block_count] * unscale[:, None, None]
    own_half = jnp.einsum(
        "ptg,pjtks->jgks",
        got_hit,
        got[..., :basis_count].astype(jnp.float32),
        precision=lax.Precision.HIGH,
        preferred_element_type=jnp.float32,
    ).reshape(occ_share, rows_here, basis_count)

    half_low = own_half.astype(jnp.bfloat16).reshape(occ_share * rows_here, basis_count)
    mixed = jnp.dot(half_low, virtual_coef, preferred_element_type=jnp.float32)
    mixed = mixed.astype(jnp.bfloat16).reshape(occ_share, rows_here, pair_count, vir_share)
    received = lax.all_to_all(mixed, "pair", split_axis=2, concat_axis=1, tiled=True)
    total_rows = received.shape[1]
    mixed_rows = received.reshape(occ_share, total_rows, vir_share)

    occ_rows = jnp.take(occupied_coef, both_index[0], axis=0, mode="clip")
    vir_rows = jnp.take(virtual_coef, both_index[1], axis=0, mode="clip")
    mixed_t = jnp.transpose(mixed_rows, (0, 2, 1))
    occ_t = jnp.transpose(occ_rows).astype(jnp.float32)
    return final_contract(mixed_t, occ_t, vir_rows)

def solution(mesh):
    placed = (
        P("pair", "lam", None, None, None),
        P("pair", "lam"),
        P("pair", "lam"),
        P("pair", "lam"),
        P("pair"),
        P("pair"),
        P(),
        P(),
    )
    return jax.shard_map(
        on_device, mesh=mesh, in_specs=placed, out_specs=P("lam", "pair", None), check_vma=False
    )
```

```python
import jax
import jax.numpy as jnp
from jax import lax
from jax.experimental import pallas as pl
from jax.experimental.pallas import tpu as pltpu
from jax.sharding import PartitionSpec as P


def contract_kernel(mixed_ref, occ_ref, vir_ref, out_ref, stack_ref):
    vir_share = mixed_ref.shape[1]
    occ_total = occ_ref.shape[0]
    vir_total = vir_ref.shape[1]
    mixed_block = mixed_ref[0].astype(jnp.float32)
    for i in range(occ_total):
        stack_ref[i * vir_share : (i + 1) * vir_share, :] = mixed_block * occ_ref[i : i + 1, :]
    product = jnp.dot(
        stack_ref[...].astype(jnp.bfloat16), vir_ref[...], preferred_element_type=jnp.float32
    )
    for i in range(occ_total):
        out_ref[0, :, i * vir_total : (i + 1) * vir_total] = product[
            i * vir_share : (i + 1) * vir_share, :
        ]


def final_contract(mixed_t, occ_t, vir_rows, interpret=False):
    occ_share, vir_share, total_rows = mixed_t.shape
    occ_total = occ_t.shape[0]
    vir_total = vir_rows.shape[1]
    return pl.pallas_call(
        contract_kernel,
        grid=(occ_share,),
        in_specs=[
            pl.BlockSpec((1, vir_share, total_rows), lambda n: (n, 0, 0)),
            pl.BlockSpec((occ_total, total_rows), lambda n: (0, 0)),
            pl.BlockSpec((total_rows, vir_total), lambda n: (0, 0)),
        ],
        out_specs=pl.BlockSpec((1, vir_share, occ_total * vir_total), lambda n: (n, 0, 0)),
        out_shape=jax.ShapeDtypeStruct((occ_share, vir_share, occ_total * vir_total), jnp.float32),
        scratch_shapes=[pltpu.VMEM((occ_total * vir_share, total_rows), jnp.float32)],
        interpret=interpret,
    )(mixed_t, occ_t, vir_rows)


def on_device(
    integrals, tile_pair, tile_lam, tile_count, mu_index, nu_index, occupied_coef, virtual_coef
):
    lam_count = lax.axis_size("lam")
    pair_count = lax.axis_size("pair")
    basis_count, occ_total = occupied_coef.shape
    vir_total = virtual_coef.shape[1]
    rows_here = mu_index.shape[0]
    occ_share = occ_total // lam_count
    vir_share = vir_total // pair_count

    index_copies = jnp.broadcast_to(
        jnp.stack([mu_index, nu_index])[None], (pair_count, 2, rows_here)
    )
    both_index = lax.all_to_all(index_copies, "pair", split_axis=0, concat_axis=0, tiled=True)
    both_index = jnp.transpose(both_index, (1, 0, 2)).reshape(2, pair_count * rows_here)

    tile_data = integrals[0]
    slot_count, tile_rows, tile_depth, _ = tile_data.shape
    block_count = rows_here // tile_rows
    pair_list = tile_pair[0]
    lam_list = tile_lam[0]
    live = jnp.arange(slot_count) < tile_count[0, 0]
    occ_blocks = occupied_coef.reshape(basis_count // tile_depth, tile_depth, occ_total)
    occ_slot = jnp.take(occ_blocks, lam_list, axis=0, mode="clip")
    occ_slot = jnp.where(live[:, None, None], occ_slot, jnp.zeros((), occ_slot.dtype))
    contrib = jnp.einsum("tmj,tkms->jtks", occ_slot, tile_data, preferred_element_type=jnp.float32)

    peak = jnp.maximum(jnp.max(jnp.abs(contrib)), 1e-30)
    exponent = jnp.clip(jnp.floor(jnp.log2(peak)), -100.0, 100.0)
    scale = jnp.exp2(13.0 - exponent)
    payload = (contrib * scale).astype(jnp.float16).reshape(
        lam_count, occ_share, slot_count, tile_rows, basis_count
    )
    hit = (pair_list[:, None] == jnp.arange(block_count)[None, :]) & live[:, None]
    info = jnp.concatenate(
        [
            hit.astype(jnp.float32),
            jnp.broadcast_to(exponent, (slot_count, 1)),
            jnp.zeros((slot_count, 128 - block_count - 1), jnp.float32),
        ],
        axis=1,
    )
    info = jnp.broadcast_to(
        info.astype(jnp.float16)[None, None, :, None, :],
        (lam_count, occ_share, slot_count, tile_rows, 128),
    )
    payload = jnp.concatenate([payload, info], axis=4)

    got = lax.all_to_all(payload, "lam", split_axis=0, concat_axis=0, tiled=True)

    got_info = got[:, 0, :, 0, basis_count:].astype(jnp.float32)
    unscale = jnp.exp2(got_info[:, 0, block_count] - 13.0)
    got_hit = got_info[:, :, :block_count] * unscale[:, None, None]
    own_half = jnp.einsum(
        "ptg,pjtks->jgks",
        got_hit,
        got[..., :basis_count].astype(jnp.float32),
        precision=lax.Precision.HIGH,
        preferred_element_type=jnp.float32,
    ).reshape(occ_share, rows_here, basis_count)

    half_low = own_half.astype(jnp.bfloat16).reshape(occ_share * rows_here, basis_count)
    mixed = jnp.dot(half_low, virtual_coef, preferred_element_type=jnp.float32)
    mixed = mixed.astype(jnp.bfloat16).reshape(occ_share, rows_here, pair_count, vir_share)
    received = lax.all_to_all(mixed, "pair", split_axis=2, concat_axis=1, tiled=True)
    total_rows = received.shape[1]
    mixed_rows = received.reshape(occ_share, total_rows, vir_share)

    occ_rows = jnp.take(occupied_coef, both_index[0], axis=0, mode="clip")
    vir_rows = jnp.take(virtual_coef, both_index[1], axis=0, mode="clip")
    mixed_t = jnp.transpose(mixed_rows, (0, 2, 1))
    occ_t = jnp.transpose(occ_rows).astype(jnp.float32)
    return final_contract(mixed_t, occ_t, vir_rows)

def solution(mesh):
    placed = (
        P("pair", "lam", None, None, None),
        P("pair", "lam"),
        P("pair", "lam"),
        P("pair", "lam"),
        P("pair"),
        P("pair"),
        P(),
        P(),
    )
    return jax.shard_map(
        on_device, mesh=mesh, in_specs=placed, out_specs=P("lam", "pair", None), check_vma=False
    )
```

```python
import jax
import jax.numpy as jnp
from jax import lax
from jax.experimental import pallas as pl
from jax.experimental.pallas import tpu as pltpu
from jax.sharding import PartitionSpec as P


def contract_kernel(mixed_ref, occ_ref, vir_ref, out_ref, stack_ref):
    vir_share = mixed_ref.shape[1]
    occ_total = occ_ref.shape[0]
    vir_total = vir_ref.shape[1]
    mixed_block = mixed_ref[0].astype(jnp.float32)
    for i in range(occ_total):
        stack_ref[i * vir_share : (i + 1) * vir_share, :] = mixed_block * occ_ref[i : i + 1, :]
    product = jnp.dot(
        stack_ref[...].astype(jnp.bfloat16), vir_ref[...], preferred_element_type=jnp.float32
    )
    for i in range(occ_total):
        out_ref[0, :, i * vir_total : (i + 1) * vir_total] = product[
            i * vir_share : (i + 1) * vir_share, :
        ]


def final_contract(mixed_t, occ_t, vir_rows, interpret=False):
    occ_share, vir_share, total_rows = mixed_t.shape
    occ_total = occ_t.shape[0]
    vir_total = vir_rows.shape[1]
    return pl.pallas_call(
        contract_kernel,
        grid=(occ_share,),
        in_specs=[
            pl.BlockSpec((1, vir_share, total_rows), lambda n: (n, 0, 0)),
            pl.BlockSpec((occ_total, total_rows), lambda n: (0, 0)),
            pl.BlockSpec((total_rows, vir_total), lambda n: (0, 0)),
        ],
        out_specs=pl.BlockSpec((1, vir_share, occ_total * vir_total), lambda n: (n, 0, 0)),
        out_shape=jax.ShapeDtypeStruct((occ_share, vir_share, occ_total * vir_total), jnp.float32),
        scratch_shapes=[pltpu.VMEM((occ_total * vir_share, total_rows), jnp.float32)],
        interpret=interpret,
    )(mixed_t, occ_t, vir_rows)


def on_device(
    integrals, tile_pair, tile_lam, tile_count, mu_index, nu_index, occupied_coef, virtual_coef
):
    lam_count = lax.axis_size("lam")
    pair_count = lax.axis_size("pair")
    basis_count, occ_total = occupied_coef.shape
    vir_total = virtual_coef.shape[1]
    rows_here = mu_index.shape[0]
    occ_share = occ_total // lam_count
    vir_share = vir_total // pair_count

    index_copies = jnp.broadcast_to(
        jnp.concatenate([mu_index, nu_index])[None], (pair_count, 2 * rows_here)
    )
    both_index = lax.all_to_all(index_copies, "pair", split_axis=0, concat_axis=0, tiled=True)
    both_index = jnp.stack(
        [both_index[:, :rows_here].reshape(-1), both_index[:, rows_here:].reshape(-1)]
    )

    tile_data = integrals[0]
    slot_count, tile_rows, tile_depth, _ = tile_data.shape
    block_count = rows_here // tile_rows
    pair_list = tile_pair[0]
    lam_list = tile_lam[0]
    live = jnp.arange(slot_count) < tile_count[0, 0]
    occ_blocks = occupied_coef.reshape(basis_count // tile_depth, tile_depth, occ_total)
    occ_slot = jnp.take(occ_blocks, lam_list, axis=0, mode="clip")
    occ_slot = jnp.where(live[:, None, None], occ_slot, jnp.zeros((), occ_slot.dtype))
    contrib = jnp.einsum("tmj,tkms->jtks", occ_slot, tile_data, preferred_element_type=jnp.float32)

    peak = jnp.maximum(jnp.max(jnp.abs(contrib)), 1e-30)
    exponent = jnp.clip(jnp.floor(jnp.log2(peak)), -100.0, 100.0)
    scale = jnp.exp2(13.0 - exponent)
    payload = (contrib * scale).astype(jnp.float16).reshape(
        lam_count, occ_share, slot_count, tile_rows, basis_count
    )
    hit = (pair_list[:, None] == jnp.arange(block_count)[None, :]) & live[:, None]
    info = jnp.concatenate(
        [
            hit.astype(jnp.float32),
            jnp.broadcast_to(exponent, (slot_count, 1)),
            jnp.zeros((slot_count, 128 - block_count - 1), jnp.float32),
        ],
        axis=1,
    )
    info = jnp.broadcast_to(
        info.astype(jnp.float16)[None, None, :, None, :],
        (lam_count, occ_share, slot_count, tile_rows, 128),
    )
    payload = jnp.concatenate([payload, info], axis=4)

    got = lax.all_to_all(payload, "lam", split_axis=0, concat_axis=0, tiled=True)

    got_info = got[:, 0, :, 0, basis_count:].astype(jnp.float32)
    unscale = jnp.exp2(got_info[:, 0, block_count] - 13.0)
    got_hit = got_info[:, :, :block_count] * unscale[:, None, None]
    own_half = jnp.einsum(
        "ptg,pjtks->jgks",
        got_hit,
        got[..., :basis_count].astype(jnp.float32),
        precision=lax.Precision.HIGH,
        preferred_element_type=jnp.float32,
    ).reshape(occ_share, rows_here, basis_count)

    half_low = own_half.astype(jnp.bfloat16).reshape(occ_share * rows_here, basis_count)
    mixed = jnp.dot(half_low, virtual_coef, preferred_element_type=jnp.float32)
    mixed = mixed.astype(jnp.bfloat16).reshape(occ_share, rows_here, pair_count, vir_share)
    received = lax.all_to_all(mixed, "pair", split_axis=2, concat_axis=1, tiled=True)
    total_rows = received.shape[1]
    mixed_rows = received.reshape(occ_share, total_rows, vir_share)

    occ_rows = jnp.take(occupied_coef, both_index[0], axis=0, mode="clip")
    vir_rows = jnp.take(virtual_coef, both_index[1], axis=0, mode="clip")
    mixed_t = jnp.transpose(mixed_rows, (0, 2, 1))
    occ_t = jnp.transpose(occ_rows).astype(jnp.float32)
    return final_contract(mixed_t, occ_t, vir_rows)

def solution(mesh):
    placed = (
        P("pair", "lam", None, None, None),
        P("pair", "lam"),
        P("pair", "lam"),
        P("pair", "lam"),
        P("pair"),
        P("pair"),
        P(),
        P(),
    )
    return jax.shard_map(
        on_device, mesh=mesh, in_specs=placed, out_specs=P("lam", "pair", None), check_vma=False
    )
```

```python
import jax
import jax.numpy as jnp
from jax import lax
from jax.experimental import pallas as pl
from jax.experimental.pallas import tpu as pltpu
from jax.sharding import PartitionSpec as P


def contract_kernel(mixed_ref, occ_ref, vir_ref, out_ref, stack_ref):
    vir_share = mixed_ref.shape[1]
    occ_total = occ_ref.shape[0]
    vir_total = vir_ref.shape[1]
    mixed_block = mixed_ref[0].astype(jnp.float32)
    for i in range(occ_total):
        stack_ref[i * vir_share : (i + 1) * vir_share, :] = mixed_block * occ_ref[i : i + 1, :]
    product = jnp.dot(
        stack_ref[...].astype(jnp.bfloat16), vir_ref[...], preferred_element_type=jnp.float32
    )
    for i in range(occ_total):
        out_ref[0, :, i * vir_total : (i + 1) * vir_total] = product[
            i * vir_share : (i + 1) * vir_share, :
        ]


def final_contract(mixed_t, occ_t, vir_rows, interpret=False):
    occ_share, vir_share, total_rows = mixed_t.shape
    occ_total = occ_t.shape[0]
    vir_total = vir_rows.shape[1]
    occ_step = occ_total // 2
    return pl.pallas_call(
        contract_kernel,
        grid=(occ_share, 2),
        in_specs=[
            pl.BlockSpec((1, vir_share, total_rows), lambda n, h: (n, 0, 0)),
            pl.BlockSpec((occ_step, total_rows), lambda n, h: (h, 0)),
            pl.BlockSpec((total_rows, vir_total), lambda n, h: (0, 0)),
        ],
        out_specs=pl.BlockSpec((1, vir_share, occ_step * vir_total), lambda n, h: (n, 0, h)),
        out_shape=jax.ShapeDtypeStruct((occ_share, vir_share, occ_total * vir_total), jnp.float32),
        scratch_shapes=[pltpu.VMEM((occ_step * vir_share, total_rows), jnp.float32)],
        interpret=interpret,
    )(mixed_t, occ_t, vir_rows)


def on_device(
    integrals, tile_pair, tile_lam, tile_count, mu_index, nu_index, occupied_coef, virtual_coef
):
    lam_count = lax.axis_size("lam")
    pair_count = lax.axis_size("pair")
    basis_count, occ_total = occupied_coef.shape
    vir_total = virtual_coef.shape[1]
    rows_here = mu_index.shape[0]
    occ_share = occ_total // lam_count
    vir_share = vir_total // pair_count

    index_copies = jnp.broadcast_to(
        jnp.stack([mu_index, nu_index])[None], (pair_count, 2, rows_here)
    )
    both_index = lax.all_to_all(index_copies, "pair", split_axis=0, concat_axis=0, tiled=True)
    both_index = jnp.transpose(both_index, (1, 0, 2)).reshape(2, pair_count * rows_here)

    tile_data = integrals[0]
    slot_count, tile_rows, tile_depth, _ = tile_data.shape
    block_count = rows_here // tile_rows
    pair_list = tile_pair[0]
    lam_list = tile_lam[0]
    live = jnp.arange(slot_count) < tile_count[0, 0]
    occ_blocks = occupied_coef.reshape(basis_count // tile_depth, tile_depth, occ_total)
    occ_slot = jnp.take(occ_blocks, lam_list, axis=0, mode="clip")
    occ_slot = jnp.where(live[:, None, None], occ_slot, jnp.zeros((), occ_slot.dtype))
    contrib = jnp.einsum("tmj,tkms->jtks", occ_slot, tile_data, preferred_element_type=jnp.float32)

    peak = jnp.maximum(jnp.max(jnp.abs(contrib)), 1e-30)
    exponent = jnp.clip(jnp.floor(jnp.log2(peak)), -100.0, 100.0)
    scale = jnp.exp2(13.0 - exponent)
    payload = (contrib * scale).astype(jnp.float16).reshape(
        lam_count, occ_share, slot_count, tile_rows, basis_count
    )
    hit = (pair_list[:, None] == jnp.arange(block_count)[None, :]) & live[:, None]
    info = jnp.concatenate(
        [
            hit.astype(jnp.float32),
            jnp.broadcast_to(exponent, (slot_count, 1)),
            jnp.zeros((slot_count, 128 - block_count - 1), jnp.float32),
        ],
        axis=1,
    )
    info = jnp.broadcast_to(
        info.astype(jnp.float16)[None, None, :, None, :],
        (lam_count, occ_share, slot_count, tile_rows, 128),
    )
    payload = jnp.concatenate([payload, info], axis=4)

    got = lax.all_to_all(payload, "lam", split_axis=0, concat_axis=0, tiled=True)

    got_info = got[:, 0, :, 0, basis_count:].astype(jnp.float32)
    unscale = jnp.exp2(got_info[:, 0, block_count] - 13.0)
    got_hit = got_info[:, :, :block_count] * unscale[:, None, None]
    own_half = jnp.einsum(
        "ptg,pjtks->jgks",
        got_hit,
        got[..., :basis_count].astype(jnp.float32),
        precision=lax.Precision.HIGH,
        preferred_element_type=jnp.float32,
    ).reshape(occ_share, rows_here, basis_count)

    half_low = own_half.astype(jnp.bfloat16).reshape(occ_share * rows_here, basis_count)
    mixed = jnp.dot(half_low, virtual_coef, preferred_element_type=jnp.float32)
    mixed = mixed.astype(jnp.bfloat16).reshape(occ_share, rows_here, pair_count, vir_share)
    received = lax.all_to_all(mixed, "pair", split_axis=2, concat_axis=1, tiled=True)
    total_rows = received.shape[1]
    mixed_rows = received.reshape(occ_share, total_rows, vir_share)

    occ_rows = jnp.take(occupied_coef, both_index[0], axis=0, mode="clip")
    vir_rows = jnp.take(virtual_coef, both_index[1], axis=0, mode="clip")
    mixed_t = jnp.transpose(mixed_rows, (0, 2, 1))
    occ_t = jnp.transpose(occ_rows).astype(jnp.float32)
    return final_contract(mixed_t, occ_t, vir_rows)

def solution(mesh):
    placed = (
        P("pair", "lam", None, None, None),
        P("pair", "lam"),
        P("pair", "lam"),
        P("pair", "lam"),
        P("pair"),
        P("pair"),
        P(),
        P(),
    )
    return jax.shard_map(
        on_device, mesh=mesh, in_specs=placed, out_specs=P("lam", "pair", None), check_vma=False
    )
```
